128 devices in a mesh: ep: 64 (over z, y, x), dp: 2 (over core).
Axes of the slice: x: 4, y: 4, z: 4, core: 2. Of those that a mesh axis runs over, the one named last changes fastest.
Arguments:
- attention_out: bfloat16 [8192, 2560], P(('ep', 'dp')), may hold values from -6 to 6
- residual: bfloat16 [8192, 2560], P(('ep', 'dp')), may hold values from -30 to 30
- out_weight: bfloat16 [2560, 2560], P(None, 'dp'), may hold values from -0.125 to 0.125
- pre_gain: float32 [2560], replicated, may hold values from 0.5 to 1.5
- routes: int32 [8192, 6], P(('ep', 'dp')), may hold values from 0 to 63, all different within a row; in each aligned block of 64 rows (0 to 63, 64 to 127, ...) at most 9 rows name the same one
- gate_prob: float32 [8192, 6], P(('ep', 'dp')), may hold values from 0.05 to 1
- gate_weight: bfloat16 [64, 2560, 1536], P('ep', None, 'dp'), may hold values from -0.125 to 0.125
- up_weight: bfloat16 [64, 2560, 1536], P('ep', None, 'dp'), may hold values from -0.125 to 0.125
- down_weight: bfloat16 [64, 1536, 2560], P('ep', None, 'dp'), may hold values from -0.15625 to 0.15625
- post_gain: float32 [2560], replicated, may hold values from 0.5 to 1.5
Outputs:
- new_state: bfloat16 [8192, 2560], P(('ep', 'dp'))
- normed_state: bfloat16 [8192, 2560], P(('ep', 'dp'))
The draws below stay inside these ranges and needn't reach their ends.
Inputs may be any that keep to these rules, and one draw needn't show every extreme that they name: `routes`: each row names 6 different experts; within the 64 rows of one device no expert is named more than 9 times, a bound that some block reaches.
All inputs are finite; a program needn't handle non-finite values.
Results may differ from the reference program's by a relative error of at most 0.015.
Values may be sent and summed in bfloat16 or wider, within the bound.
No kernel may reach another device: no remote copies, remote signals or barrier semaphores. Data moves between devices by JAX's collectives and lax.ppermute only.
A program may use at most 128 MiB of HBM per device.

```python
import math
import jax
import jax.numpy as jnp
import numpy as np
from jax import lax

D = 2560
FF = 1536
TOP = 6
TOK_DEV = 64
ATT = 2560
EXPERTS = 64
CAP = 9
TOKENS = 8192
N_EP = 64
N_DP = 2


def draw_residual(key, part):
    first_key, second_key = jax.random.split(key)
    scales = jnp.exp(jax.random.uniform(first_key, (TOKENS, 1), jnp.float32, math.log(0.3), math.log(3.0)))
    base = jnp.clip(jax.random.normal(second_key, (TOKENS, D), jnp.float32), -6.0, 6.0)
    return (scales * base).astype(jnp.bfloat16)


def block_levels(rng, extent, cuts, smallest, high):
    def one(axis_at, shards_of):
        draws = jax.random.uniform(jax.random.fold_in(jax.random.fold_in(rng, 6), axis_at), (shards_of,), jnp.float32, smallest / len(cuts), high / len(cuts))
        return jnp.repeat(jnp.exp(draws), extent[axis_at] // shards_of).reshape((-1,) + (1,) * (len(extent) - axis_at - 1))

    loudness = one(*cuts[0])
    for cut in cuts[1:]:
        loudness = loudness * one(*cut)
    return loudness


def shared_out(stream_key, own, number, rows, count, top, limit, skew):
    ranking = jax.random.permutation(stream_key, count)
    heavy_load, common = load_shares(count, rows * top, limit, skew, True), load_shares(count, rows * top, limit, skew, False)
    places = jnp.arange(count)

    def named(lengths, turn):
        used = int((lengths > 0).sum())
        fixed = max(1, used // 4)
        passed = fixed + (places - fixed + turn * (used - fixed)) % max(1, count - fixed)
        return jnp.zeros((count,), jnp.int32).at[ranking[jnp.where(places < fixed, places, passed)]].set(jnp.asarray(lengths, jnp.int32))

    lengths = jnp.where(number % 4 == 0, named(heavy_load, number // 4), named(common, number - number // 4 - 1))
    mixed = jax.random.permutation(jax.random.fold_in(own, 3), count)
    source_of, taker = mixed[0:count // 2 * 2:2], mixed[1:count // 2 * 2:2]
    slack = jnp.minimum(lengths[source_of] - 1, limit - lengths[taker]) // 2
    slack = jnp.where((source_of == ranking[0]) | (taker == ranking[0]) | (lengths[taker] == 0), 0, jnp.maximum(slack, 0))
    passed = jax.random.randint(jax.random.fold_in(own, 4), (count // 2,), 0, 1 << 20) % (slack + 1)
    lengths = lengths.at[source_of].add(-passed).at[taker].add(passed)
    labels = jnp.searchsorted(jnp.cumsum(lengths), jnp.arange(rows * top), side="right").astype(jnp.int32)
    grid = labels.reshape(top, rows).T
    grid = grid[jax.random.permutation(jax.random.fold_in(own, 1), rows)]
    turn = jax.random.randint(jax.random.fold_in(own, 2), (rows, 1), 0, top)
    return jnp.take_along_axis(grid, (jnp.arange(top)[None, :] + turn) % top, axis=1)


def load_shares(amount, total, limit, skew, full):
    loads = [(1 << 20) // math.isqrt(grade ** skew) + 1 for grade in range(1, amount + 1)]
    largest = limit if full else min(limit, max(-(-total // amount), total * loads[0] // sum(loads)))
    least = 1 if total - largest >= amount - 1 else 0
    holding, rest = [largest] + [least] * (amount - 1), total - largest - least * (amount - 1)
    while rest > 0:
        candidates = [i for i in range(1, amount) if holding[i] < largest] or [i for i in range(1, amount) if holding[i] < limit]
        whole, remaining = sum([loads[i] for i in candidates]), rest
        for i in candidates:
            more = min(limit - holding[i], max(1, remaining * loads[i] // whole), rest)
            holding[i] = holding[i] + more
            rest = rest - more
    return np.array(holding)


def normal_values(stream_key, extent, scale, limit, pieces=(), kind=jnp.bfloat16):
    values = jax.random.normal(stream_key, extent, jnp.float32) * scale
    if len(pieces) > 0:
        values = block_levels(stream_key, extent, pieces, -0.22, 0.18) * values
    return jnp.clip(values, min=-limit, max=limit).astype(kind)


def setup_inputs(seed: int = 0) -> dict:
    keys = jax.random.split(jax.random.key(seed), 11)
    attention_out = normal_values(keys[0], (TOKENS, ATT), 1.0, 6.0, ((0, 128),))
    residual = draw_residual(jax.random.fold_in(keys[10], 71), 0)
    out_weight = normal_values(keys[2], (ATT, D), ATT ** -0.5, 0.125, ((1, 2),))
    pre_gain = jnp.clip(1.0 + 0.1 * jax.random.normal(keys[3], (D,), jnp.float32), 0.5, 1.5)
    routes_keys = jax.random.split(jax.random.fold_in(keys[4], 1), TOKENS // TOK_DEV)
    routes_turns = jax.random.permutation(jax.random.fold_in(keys[4], 3), TOKENS // TOK_DEV)
    routes = jax.vmap(lambda own, number: shared_out(jax.random.fold_in(keys[4], 2), own, number, TOK_DEV, EXPERTS, TOP, CAP, 2))(routes_keys, routes_turns).reshape((TOKENS, TOP))
    gate_prob = jnp.clip(jnp.exp(math.log(1.0) - 2.9957323 * jax.random.uniform(keys[5], (TOKENS, TOP), jnp.float32) ** block_levels(keys[5], (TOKENS, TOP), ((0, 128),), -0.2, 0.2)), 0.05, 1.0)
    gate_weight = normal_values(keys[6], (EXPERTS, D, FF), D ** -0.5, 0.125, ((0, 64), (2, 2)))
    up_weight = normal_values(keys[7], (EXPERTS, D, FF), D ** -0.5, 0.125, ((0, 64), (2, 2)))
    down_weight = normal_values(keys[8], (EXPERTS, FF, D), FF ** -0.5, 0.15625, ((0, 64), (2, 2)))
    post_gain = jnp.clip(1.0 + 0.1 * jax.random.normal(keys[9], (D,), jnp.float32), 0.5, 1.5)
    return dict(attention_out=attention_out, residual=residual, out_weight=out_weight, pre_gain=pre_gain, routes=routes, gate_prob=gate_prob, gate_weight=gate_weight, up_weight=up_weight, down_weight=down_weight, post_gain=post_gain)


def rms_scale(values, gain):
    widened = values.astype(jnp.float32)
    meansq = lax.optimization_barrier(jnp.mean(widened * widened, axis=-1, keepdims=True))
    return widened * lax.rsqrt(meansq + 1e-06) * gain

def slot_table(route_block, experts, capacity):
    flat_ids = route_block.reshape(-1)
    onehot = (flat_ids[:, None] == jnp.arange(experts, dtype=jnp.int32)[None, :]).astype(jnp.int32)
    before = jnp.cumsum(onehot, axis=0) - onehot
    rank_in = lax.optimization_barrier(jnp.sum(before * onehot, axis=1))
    return (flat_ids * capacity + rank_in).reshape(route_block.shape)

def reference(attention_out, residual, out_weight, pre_gain, routes, gate_prob, gate_weight, up_weight, down_weight, post_gain):
    proj = jnp.dot(attention_out, out_weight, preferred_element_type=jnp.float32)
    summed = (residual.astype(jnp.float32) + proj).astype(jnp.bfloat16)
    normed_in = rms_scale(summed, pre_gain).astype(jnp.bfloat16)
    dev_count = N_EP * N_DP
    blocks = routes.reshape(dev_count, TOK_DEV, TOP)
    slot_ids = jax.vmap(lambda blk: slot_table(blk, EXPERTS, CAP))(blocks)
    expert_ids = slot_ids // CAP
    rank_in = slot_ids % CAP
    device_ids = jnp.arange(dev_count, dtype=jnp.int32)[:, None, None]
    position = (device_ids * CAP + rank_in).astype(jnp.int32)
    token_ids = device_ids * TOK_DEV + jnp.arange(TOK_DEV, dtype=jnp.int32)[None, :, None]
    token_ids = jnp.broadcast_to(token_ids, slot_ids.shape).astype(jnp.int32)
    buffer_ids = jnp.full((EXPERTS, dev_count * CAP), TOKENS, jnp.int32)
    buffer_ids = buffer_ids.at[expert_ids, position].set(token_ids)
    padded = jnp.concatenate([normed_in, jnp.zeros((1, D), jnp.bfloat16)], axis=0)

    def run_expert(index):
        rows_in = padded[buffer_ids[index]]
        gate_part = jnp.dot(rows_in, gate_weight[index], preferred_element_type=jnp.float32)
        up_part = jnp.dot(rows_in, up_weight[index], preferred_element_type=jnp.float32)
        hidden = (jax.nn.silu(gate_part) * up_part).astype(jnp.bfloat16)
        return jnp.dot(hidden, down_weight[index], preferred_element_type=jnp.float32).astype(jnp.bfloat16)
    results = lax.map(run_expert, jnp.arange(EXPERTS, dtype=jnp.int32))
    weight = gate_prob / lax.optimization_barrier(jnp.sum(gate_prob, axis=1, keepdims=True))
    picked = results[expert_ids.reshape(TOKENS, TOP), position.reshape(TOKENS, TOP)]
    expert_sum = jnp.einsum('tk,tkd->td', weight.astype(jnp.float32), picked.astype(jnp.float32), precision=lax.Precision.HIGHEST)
    new_state = (summed.astype(jnp.float32) + expert_sum).astype(jnp.bfloat16)
    normed_state = rms_scale(new_state, post_gain).astype(jnp.bfloat16)
    return (new_state, normed_state)
```

```python
import jax
import jax.numpy as jnp
from jax import lax
from jax.sharding import PartitionSpec as P


def rms_scale(values, gain):
    widened = values.astype(jnp.float32)
    meansq = jnp.mean(widened * widened, axis=-1, keepdims=True)
    return widened * lax.rsqrt(meansq + 1e-06) * gain


def slot_table(route_block, experts, capacity):
    flat_ids = route_block.reshape(-1)
    onehot = (flat_ids[:, None] == jnp.arange(experts, dtype=jnp.int32)[None, :]).astype(jnp.int32)
    before = jnp.cumsum(onehot, axis=0) - onehot
    rank_in = jnp.sum(before * onehot, axis=1)
    return (flat_ids * capacity + rank_in).reshape(route_block.shape)


def exchange_rows(rows, experts):
    total, width = rows.shape
    lanes = 128
    wire = rows.reshape(experts, total * width // (experts * lanes), lanes)
    moved = lax.all_to_all(wire, "ep", split_axis=0, concat_axis=0, tiled=True)
    return moved.reshape(total, width)


def per_device(
    attention_out,
    residual,
    out_weight,
    pre_gain,
    routes,
    gate_prob,
    gate_weight,
    up_weight,
    down_weight,
    post_gain,
):
    groups = lax.axis_size("dp")
    experts = lax.axis_size("ep")
    tok_rows, top_picks = routes.shape
    row_width = residual.shape[1]
    part_cols = out_weight.shape[1]
    capacity = max(2, 3 * tok_rows * top_picks // (2 * experts))
    columns = jnp.dot(
        lax.all_gather(attention_out, "dp", axis=0, tiled=True),
        out_weight,
        preferred_element_type=jnp.float32,
    )
    home_cols = lax.all_to_all(
        columns.reshape(groups, tok_rows, part_cols).astype(jnp.bfloat16),
        "dp",
        split_axis=0,
        concat_axis=2,
        tiled=True,
    ).astype(jnp.float32)
    summed = (residual.astype(jnp.float32) + home_cols.reshape(tok_rows, row_width)).astype(
        jnp.bfloat16
    )
    normed_in = rms_scale(summed, pre_gain).astype(jnp.bfloat16)
    slot_ids = slot_table(routes, experts, capacity)
    matches = (
        slot_ids[:, :, None] == jnp.arange(experts * capacity, dtype=jnp.int32)[None, None, :]
    ).astype(jnp.float32)
    placing = jnp.sum(matches, axis=1).astype(jnp.bfloat16)
    weights = gate_prob / jnp.sum(gate_prob, axis=1, keepdims=True)
    mixing = jnp.sum(weights[:, :, None] * matches, axis=1)
    outgoing = lax.dot_general(
        placing, normed_in, (((0,), (0,)), ((), ())), preferred_element_type=jnp.float32
    ).astype(jnp.bfloat16)
    gate_local = gate_weight[0]
    up_local = up_weight[0]
    down_local = down_weight[0]
    arrived = exchange_rows(outgoing, experts)
    segment = lax.all_gather(arrived, "dp", axis=0, tiled=True)
    gate_part = jnp.dot(segment, gate_local, preferred_element_type=jnp.float32)
    up_part = jnp.dot(segment, up_local, preferred_element_type=jnp.float32)
    hidden = (jax.nn.silu(gate_part) * up_part).astype(jnp.bfloat16)
    results = jnp.dot(
        lax.all_gather(hidden, "dp", axis=1, tiled=True),
        down_local,
        preferred_element_type=jnp.float32,
    ).astype(jnp.bfloat16)
    joined = lax.all_to_all(
        results.reshape(groups, experts * capacity, part_cols),
        "dp",
        split_axis=0,
        concat_axis=2,
        tiled=True,
    )
    returned = exchange_rows(joined.reshape(experts * capacity, row_width), experts).astype(
        jnp.float32
    )
    expert_sum = jnp.dot(
        mixing, returned, precision=lax.Precision.HIGHEST, preferred_element_type=jnp.float32
    )
    new_state = (summed.astype(jnp.float32) + expert_sum).astype(jnp.bfloat16)
    normed_state = rms_scale(new_state, post_gain).astype(jnp.bfloat16)
    return (new_state, normed_state)


def solution(mesh):
    return jax.shard_map(
        per_device,
        mesh=mesh,
        in_specs=(
            P(("ep", "dp"), None),
            P(("ep", "dp"), None),
            P(None, "dp"),
            P(),
            P(("ep", "dp"), None),
            P(("ep", "dp"), None),
            P("ep", None, "dp"),
            P("ep", None, "dp"),
            P("ep", None, "dp"),
            P(),
        ),
        out_specs=(P(("ep", "dp"), None), P(("ep", "dp"), None)),
        check_vma=False,
    )
```

```python
import jax
import jax.numpy as jnp
from jax import lax
from jax.sharding import PartitionSpec as P


def rms_scale(values, gain):
    widened = values.astype(jnp.float32)
    meansq = jnp.mean(widened * widened, axis=-1, keepdims=True)
    return widened * lax.rsqrt(meansq + 1e-06) * gain


def slot_table(route_block, experts, capacity):
    flat_ids = route_block.reshape(-1)
    onehot = (flat_ids[:, None] == jnp.arange(experts, dtype=jnp.int32)[None, :]).astype(jnp.int32)
    before = jnp.cumsum(onehot, axis=0) - onehot
    rank_in = jnp.sum(before * onehot, axis=1)
    return (flat_ids * capacity + rank_in).reshape(route_block.shape)


def exchange_rows(rows, experts):
    total, width = rows.shape
    lanes = 128
    wire = rows.reshape(experts, total * width // (experts * lanes), lanes)
    moved = lax.all_to_all(wire, "ep", split_axis=0, concat_axis=0, tiled=True)
    return moved.reshape(total, width)


def per_device(
    attention_out,
    residual,
    out_weight,
    pre_gain,
    routes,
    gate_prob,
    gate_weight,
    up_weight,
    down_weight,
    post_gain,
):
    groups = lax.axis_size("dp")
    experts = lax.axis_size("ep")
    tok_rows, top_picks = routes.shape
    row_width = residual.shape[1]
    part_cols = out_weight.shape[1]
    capacity = max(2, 3 * tok_rows * top_picks // (2 * experts))
    columns = jnp.dot(
        lax.all_gather(attention_out, "dp", axis=0, tiled=True),
        out_weight,
        preferred_element_type=jnp.float32,
    )
    home_cols = lax.all_to_all(
        columns.reshape(groups, tok_rows, part_cols).astype(jnp.bfloat16),
        "dp",
        split_axis=0,
        concat_axis=2,
        tiled=True,
    ).astype(jnp.float32)
    summed = (residual.astype(jnp.float32) + home_cols.reshape(tok_rows, row_width)).astype(
        jnp.bfloat16
    )
    normed_in = rms_scale(summed, pre_gain).astype(jnp.bfloat16)
    slot_ids = slot_table(routes, experts, capacity)
    matches = (
        slot_ids[:, :, None] == jnp.arange(experts * capacity, dtype=jnp.int32)[None, None, :]
    ).astype(jnp.float32)
    placing = jnp.sum(matches, axis=1).astype(jnp.bfloat16)
    weights = gate_prob / jnp.sum(gate_prob, axis=1, keepdims=True)
    mixing = jnp.sum(weights[:, :, None] * matches, axis=1)
    outgoing = lax.dot_general(
        placing, normed_in, (((0,), (0,)), ((), ())), preferred_element_type=jnp.float32
    ).astype(jnp.bfloat16)
    gate_local = gate_weight[0]
    up_local = up_weight[0]
    down_local = down_weight[0]
    swap = [(0, 1), (1, 0)]
    own_rows = exchange_rows(outgoing, experts)
    other_rows = lax.ppermute(own_rows, "dp", swap)

    def hidden_of(rows):
        gate_part = jnp.dot(rows, gate_local, preferred_element_type=jnp.float32)
        up_part = jnp.dot(rows, up_local, preferred_element_type=jnp.float32)
        return (jax.nn.silu(gate_part) * up_part).astype(jnp.bfloat16)

    hidden_own = hidden_of(own_rows)
    hidden_own_in = lax.ppermute(hidden_own, "dp", swap)
    hidden_other = hidden_of(other_rows)
    hidden_other_in = lax.ppermute(hidden_other, "dp", swap)
    me = lax.axis_index("dp")

    ff_half = hidden_own.shape[1]
    down_mine = lax.dynamic_slice_in_dim(down_local, me * ff_half, ff_half, axis=0)
    down_theirs = lax.dynamic_slice_in_dim(down_local, (1 - me) * ff_half, ff_half, axis=0)

    def project(mine, theirs):
        total = jnp.dot(mine, down_mine, preferred_element_type=jnp.float32)
        total = total + jnp.dot(theirs, down_theirs, preferred_element_type=jnp.float32)
        return total.astype(jnp.bfloat16)

    out_other = project(hidden_other, hidden_own_in)
    out_other_in = lax.ppermute(out_other, "dp", swap)
    out_own = project(hidden_own, hidden_other_in)
    joined = jnp.concatenate([out_own, out_other_in], axis=1)
    returned = exchange_rows(joined, experts).astype(jnp.float32)
    expert_sum = jnp.dot(
        mixing, returned, precision=lax.Precision.HIGHEST, preferred_element_type=jnp.float32
    )
    expert_sum = jnp.where(me == 0, expert_sum, jnp.roll(expert_sum, part_cols, axis=1))
    new_state = (summed.astype(jnp.float32) + expert_sum).astype(jnp.bfloat16)
    normed_state = rms_scale(new_state, post_gain).astype(jnp.bfloat16)
    return (new_state, normed_state)


def solution(mesh):
    return jax.shard_map(
        per_device,
        mesh=mesh,
        in_specs=(
            P(("ep", "dp"), None),
            P(("ep", "dp"), None),
            P(None, "dp"),
            P(),
            P(("ep", "dp"), None),
            P(("ep", "dp"), None),
            P("ep", None, "dp"),
            P("ep", None, "dp"),
            P("ep", None, "dp"),
            P(),
        ),
        out_specs=(P(("ep", "dp"), None), P(("ep", "dp"), None)),
        check_vma=False,
    )
```

```python
import jax
import jax.numpy as jnp
from jax import lax
from jax.sharding import PartitionSpec as P


def rms_scale(values, gain):
    widened = values.astype(jnp.float32)
    meansq = jnp.mean(widened * widened, axis=-1, keepdims=True)
    return widened * lax.rsqrt(meansq + 1e-06) * gain


def slot_table(route_block, experts, capacity):
    flat_ids = route_block.reshape(-1)
    onehot = (flat_ids[:, None] == jnp.arange(experts, dtype=jnp.int32)[None, :]).astype(jnp.int32)
    before = jnp.cumsum(onehot, axis=0) - onehot
    rank_in = jnp.sum(before * onehot, axis=1)
    return (flat_ids * capacity + rank_in).reshape(route_block.shape)


def exchange_rows(rows, experts):
    total, width = rows.shape
    lanes = 128
    wire = rows.reshape(experts, total * width // (experts * lanes), lanes)
    moved = lax.all_to_all(wire, "ep", split_axis=0, concat_axis=0, tiled=True)
    return moved.reshape(total, width)


def per_device(
    attention_out,
    residual,
    out_weight,
    pre_gain,
    routes,
    gate_prob,
    gate_weight,
    up_weight,
    down_weight,
    post_gain,
):
    groups = lax.axis_size("dp")
    experts = lax.axis_size("ep")
    tok_rows, top_picks = routes.shape
    row_width = residual.shape[1]
    part_cols = out_weight.shape[1]
    capacity = max(2, 3 * tok_rows * top_picks // (2 * experts))
    columns = jnp.dot(
        lax.all_gather(attention_out, "dp", axis=0, tiled=True),
        out_weight,
        preferred_element_type=jnp.float32,
    )
    home_cols = lax.all_to_all(
        columns.reshape(groups, tok_rows, part_cols).astype(jnp.bfloat16),
        "dp",
        split_axis=0,
        concat_axis=2,
        tiled=True,
    ).astype(jnp.float32)
    summed = (residual.astype(jnp.float32) + home_cols.reshape(tok_rows, row_width)).astype(
        jnp.bfloat16
    )
    normed_in = rms_scale(summed, pre_gain).astype(jnp.bfloat16)
    slot_ids = slot_table(routes, experts, capacity)
    matches = (
        slot_ids[:, :, None] == jnp.arange(experts * capacity, dtype=jnp.int32)[None, None, :]
    ).astype(jnp.float32)
    placing = jnp.sum(matches, axis=1).astype(jnp.bfloat16)
    weights = gate_prob / jnp.sum(gate_prob, axis=1, keepdims=True)
    mixing = jnp.sum(weights[:, :, None] * matches, axis=1)
    gate_local = gate_weight[0]
    up_local = up_weight[0]
    down_local = down_weight[0]
    swap = [(0, 1), (1, 0)]
    me = lax.axis_index("dp")
    ff_half = gate_local.shape[1]
    down_mine = lax.dynamic_slice_in_dim(down_local, me * ff_half, ff_half, axis=0)
    down_theirs = lax.dynamic_slice_in_dim(down_local, (1 - me) * ff_half, ff_half, axis=0)

    def hidden_of(rows):
        gate_part = jnp.dot(rows, gate_local, preferred_element_type=jnp.float32)
        up_part = jnp.dot(rows, up_local, preferred_element_type=jnp.float32)
        return (jax.nn.silu(gate_part) * up_part).astype(jnp.bfloat16)

    def project(mine, theirs):
        total = jnp.dot(mine, down_mine, preferred_element_type=jnp.float32)
        total = total + jnp.dot(theirs, down_theirs, preferred_element_type=jnp.float32)
        return total.astype(jnp.bfloat16)

    def expert_rows(own_rows):
        other_rows = lax.ppermute(own_rows, "dp", swap)
        hidden_own = hidden_of(own_rows)
        hidden_own_in = lax.ppermute(hidden_own, "dp", swap)
        hidden_other = hidden_of(other_rows)
        hidden_other_in = lax.ppermute(hidden_other, "dp", swap)
        out_other = project(hidden_other, hidden_own_in)
        out_other_in = lax.ppermute(out_other, "dp", swap)
        out_own = project(hidden_own, hidden_other_in)
        return jnp.concatenate([out_own, out_other_in], axis=1)

    placing3 = placing.reshape(tok_rows, experts, capacity)
    mixing3 = mixing.reshape(tok_rows, experts, capacity)
    cut = (capacity + 1) // 2
    expert_sum = None
    for lo, hi in ((0, cut), (cut, capacity)):
        chunk_place = placing3[:, :, lo:hi].reshape(tok_rows, -1)
        outgoing = lax.dot_general(
            chunk_place, normed_in, (((0,), (0,)), ((), ())), preferred_element_type=jnp.float32
        ).astype(jnp.bfloat16)
        joined = expert_rows(exchange_rows(outgoing, experts))
        returned = exchange_rows(joined, experts).astype(jnp.float32)
        part = jnp.dot(
            mixing3[:, :, lo:hi].reshape(tok_rows, -1),
            returned,
            precision=lax.Precision.HIGHEST,
            preferred_element_type=jnp.float32,
        )
        expert_sum = part if expert_sum is None else expert_sum + part
    expert_sum = jnp.where(me == 0, expert_sum, jnp.roll(expert_sum, part_cols, axis=1))
    new_state = (summed.astype(jnp.float32) + expert_sum).astype(jnp.bfloat16)
    normed_state = rms_scale(new_state, post_gain).astype(jnp.bfloat16)
    return (new_state, normed_state)


def solution(mesh):
    return jax.shard_map(
        per_device,
        mesh=mesh,
        in_specs=(
            P(("ep", "dp"), None),
            P(("ep", "dp"), None),
            P(None, "dp"),
            P(),
            P(("ep", "dp"), None),
            P(("ep", "dp"), None),
            P("ep", None, "dp"),
            P("ep", None, "dp"),
            P("ep", None, "dp"),
            P(),
        ),
        out_specs=(P(("ep", "dp"), None), P(("ep", "dp"), None)),
        check_vma=False,
    )
```

```python
import jax
import jax.numpy as jnp
from jax import lax
from jax.sharding import PartitionSpec as P


def rms_scale(values, gain):
    widened = values.astype(jnp.float32)
    meansq = jnp.mean(widened * widened, axis=-1, keepdims=True)
    return widened * lax.rsqrt(meansq + 1e-06) * gain


def slot_table(route_block, experts, capacity):
    flat_ids = route_block.reshape(-1)
    onehot = (flat_ids[:, None] == jnp.arange(experts, dtype=jnp.int32)[None, :]).astype(jnp.int32)
    before = jnp.cumsum(onehot, axis=0) - onehot
    rank_in = jnp.sum(before * onehot, axis=1)
    return (flat_ids * capacity + rank_in).reshape(route_block.shape)


def exchange_rows(rows, experts):
    total, width = rows.shape
    lanes = 128
    wire = rows.reshape(experts, total * width // (experts * lanes), lanes)
    moved = lax.all_to_all(wire, "ep", split_axis=0, concat_axis=0, tiled=True)
    return moved.reshape(total, width)


def per_device(
    attention_out,
    residual,
    out_weight,
    pre_gain,
    routes,
    gate_prob,
    gate_weight,
    up_weight,
    down_weight,
    post_gain,
):
    groups = lax.axis_size("dp")
    experts = lax.axis_size("ep")
    tok_rows, top_picks = routes.shape
    row_width = residual.shape[1]
    part_cols = out_weight.shape[1]
    capacity = max(2, 3 * tok_rows * top_picks // (2 * experts))
    swap = [(0, 1), (1, 0)]
    me = lax.axis_index("dp")
    partner_att = lax.ppermute(attention_out, "dp", swap)
    cols_own = jnp.dot(attention_out, out_weight, preferred_element_type=jnp.float32)
    cols_partner = jnp.dot(partner_att, out_weight, preferred_element_type=jnp.float32)
    cols_in = lax.ppermute(cols_partner.astype(jnp.bfloat16), "dp", swap).astype(jnp.float32)
    home_cols = jnp.where(
        me == 0,
        jnp.concatenate([cols_own, cols_in], axis=1),
        jnp.concatenate([cols_in, cols_own], axis=1),
    )
    summed = (residual.astype(jnp.float32) + home_cols).astype(jnp.bfloat16)
    normed_in = rms_scale(summed, pre_gain).astype(jnp.bfloat16)
    slot_ids = slot_table(routes, experts, capacity)
    matches = (
        slot_ids[:, :, None] == jnp.arange(experts * capacity, dtype=jnp.int32)[None, None, :]
    ).astype(jnp.float32)
    placing = jnp.sum(matches, axis=1).astype(jnp.bfloat16)
    weights = gate_prob / jnp.sum(gate_prob, axis=1, keepdims=True)
    mixing = jnp.sum(weights[:, :, None] * matches, axis=1)
    outgoing = lax.dot_general(
        placing, normed_in, (((0,), (0,)), ((), ())), preferred_element_type=jnp.float32
    ).astype(jnp.bfloat16)
    gate_local = gate_weight[0]
    up_local = up_weight[0]
    down_local = down_weight[0]
    own_rows = exchange_rows(outgoing, experts)
    other_rows = lax.ppermute(own_rows, "dp", swap)

    def hidden_of(rows):
        gate_part = jnp.dot(rows, gate_local, preferred_element_type=jnp.float32)
        up_part = jnp.dot(rows, up_local, preferred_element_type=jnp.float32)
        return (jax.nn.silu(gate_part) * up_part).astype(jnp.bfloat16)

    hidden_own = hidden_of(own_rows)
    hidden_own_in = lax.ppermute(hidden_own, "dp", swap)
    hidden_other = hidden_of(other_rows)
    hidden_other_in = lax.ppermute(hidden_other, "dp", swap)
    me = lax.axis_index("dp")

    ff_half = hidden_own.shape[1]
    down_mine = lax.dynamic_slice_in_dim(down_local, me * ff_half, ff_half, axis=0)
    down_theirs = lax.dynamic_slice_in_dim(down_local, (1 - me) * ff_half, ff_half, axis=0)

    def project(mine, theirs):
        total = jnp.dot(mine, down_mine, preferred_element_type=jnp.float32)
        total = total + jnp.dot(theirs, down_theirs, preferred_element_type=jnp.float32)
        return total.astype(jnp.bfloat16)

    out_other = project(hidden_other, hidden_own_in)
    out_other_in = lax.ppermute(out_other, "dp", swap)
    out_own = project(hidden_own, hidden_other_in)
    joined = jnp.concatenate([out_own, out_other_in], axis=1)
    returned = exchange_rows(joined, experts)
    mixing_hi = mixing.astype(jnp.bfloat16)
    mixing_lo = (mixing - mixing_hi.astype(jnp.float32)).astype(jnp.bfloat16)
    expert_sum = jnp.dot(mixing_hi, returned, preferred_element_type=jnp.float32)
    expert_sum = expert_sum + jnp.dot(mixing_lo, returned, preferred_element_type=jnp.float32)
    expert_sum = jnp.where(me == 0, expert_sum, jnp.roll(expert_sum, part_cols, axis=1))
    new_state = (summed.astype(jnp.float32) + expert_sum).astype(jnp.bfloat16)
    normed_state = rms_scale(new_state, post_gain).astype(jnp.bfloat16)
    return (new_state, normed_state)


def solution(mesh):
    return jax.shard_map(
        per_device,
        mesh=mesh,
        in_specs=(
            P(("ep", "dp"), None),
            P(("ep", "dp"), None),
            P(None, "dp"),
            P(),
            P(("ep", "dp"), None),
            P(("ep", "dp"), None),
            P("ep", None, "dp"),
            P("ep", None, "dp"),
            P("ep", None, "dp"),
            P(),
        ),
        out_specs=(P(("ep", "dp"), None), P(("ep", "dp"), None)),
        check_vma=False,
    )
```

```python
import jax
import jax.numpy as jnp
from jax import lax
from jax.sharding import PartitionSpec as P


def rms_scale(values, gain):
    widened = values.astype(jnp.float32)
    meansq = jnp.mean(widened * widened, axis=-1, keepdims=True)
    return widened * lax.rsqrt(meansq + 1e-06) * gain


def slot_table(route_block, experts, capacity):
    flat_ids = route_block.reshape(-1)
    onehot = (flat_ids[:, None] == jnp.arange(experts, dtype=jnp.int32)[None, :]).astype(jnp.int32)
    before = jnp.cumsum(onehot, axis=0) - onehot
    rank_in = jnp.sum(before * onehot, axis=1)
    return (flat_ids * capacity + rank_in).reshape(route_block.shape)


def exchange_rows(rows, experts):
    total, width = rows.shape
    lanes = 128
    wire = rows.reshape(experts, total * width // (experts * lanes), lanes)
    moved = lax.all_to_all(wire, "ep", split_axis=0, concat_axis=0, tiled=True)
    return moved.reshape(total, width)


def return_rows(first, second, experts):
    total, width = first.shape
    lanes = 128
    cut = total * width // (experts * lanes)
    wire = jnp.zeros((experts, 2 * cut, lanes), first.dtype)
    wire = wire.at[:, :cut].set(first.reshape(experts, cut, lanes))
    wire = wire.at[:, cut:].set(second.reshape(experts, cut, lanes))
    moved = lax.all_to_all(wire, "ep", split_axis=0, concat_axis=0, tiled=True)
    return [moved[:, :cut].reshape(total, width), moved[:, cut:].reshape(total, width)]


def per_device(
    attention_out,
    residual,
    out_weight,
    pre_gain,
    routes,
    gate_prob,
    gate_weight,
    up_weight,
    down_weight,
    post_gain,
):
    groups = lax.axis_size("dp")
    experts = lax.axis_size("ep")
    tok_rows, top_picks = routes.shape
    row_width = residual.shape[1]
    part_cols = out_weight.shape[1]
    capacity = max(2, 3 * tok_rows * top_picks // (2 * experts))
    swap = [(0, 1), (1, 0)]
    me = lax.axis_index("dp")
    partner_att = lax.ppermute(attention_out, "dp", swap)
    cols_own = jnp.dot(attention_out, out_weight, preferred_element_type=jnp.float32)
    cols_partner = jnp.dot(partner_att, out_weight, preferred_element_type=jnp.float32)
    cols_in = lax.ppermute(cols_partner.astype(jnp.bfloat16), "dp", swap).astype(jnp.float32)
    home_cols = jnp.where(
        me == 0,
        jnp.concatenate([cols_own, cols_in], axis=1),
        jnp.concatenate([cols_in, cols_own], axis=1),
    )
    summed = (residual.astype(jnp.float32) + home_cols).astype(jnp.bfloat16)
    normed_in = rms_scale(summed, pre_gain).astype(jnp.bfloat16)
    slot_ids = slot_table(routes, experts, capacity)
    matches = (
        slot_ids[:, :, None] == jnp.arange(experts * capacity, dtype=jnp.int32)[None, None, :]
    ).astype(jnp.float32)
    placing = jnp.sum(matches, axis=1).astype(jnp.bfloat16)
    weights = gate_prob / jnp.sum(gate_prob, axis=1, keepdims=True)
    mixing = jnp.sum(weights[:, :, None] * matches, axis=1)
    outgoing = lax.dot_general(
        placing, normed_in, (((0,), (0,)), ((), ())), preferred_element_type=jnp.float32
    ).astype(jnp.bfloat16)
    gate_local = gate_weight[0]
    up_local = up_weight[0]
    down_local = down_weight[0]
    own_rows = exchange_rows(outgoing, experts)
    other_rows = lax.ppermute(own_rows, "dp", swap)

    def hidden_of(rows):
        gate_part = jnp.dot(rows, gate_local, preferred_element_type=jnp.float32)
        up_part = jnp.dot(rows, up_local, preferred_element_type=jnp.float32)
        return (jax.nn.silu(gate_part) * up_part).astype(jnp.bfloat16)

    hidden_own = hidden_of(own_rows)
    hidden_own_in = lax.ppermute(hidden_own, "dp", swap)
    hidden_other = hidden_of(other_rows)
    hidden_other_in = lax.ppermute(hidden_other, "dp", swap)
    me = lax.axis_index("dp")

    ff_half = hidden_own.shape[1]
    down_mine = lax.dynamic_slice_in_dim(down_local, me * ff_half, ff_half, axis=0)
    down_theirs = lax.dynamic_slice_in_dim(down_local, (1 - me) * ff_half, ff_half, axis=0)

    def project(mine, theirs):
        total = jnp.dot(mine, down_mine, preferred_element_type=jnp.float32)
        total = total + jnp.dot(theirs, down_theirs, preferred_element_type=jnp.float32)
        return total.astype(jnp.bfloat16)

    out_other = project(hidden_other, hidden_own_in)
    out_other_in = lax.ppermute(out_other, "dp", swap)
    out_own = project(hidden_own, hidden_other_in)
    returned = return_rows(out_own, out_other_in, experts)
    mixing_hi = mixing.astype(jnp.bfloat16)
    mixing_lo = (mixing - mixing_hi.astype(jnp.float32)).astype(jnp.bfloat16)
    sums = []
    for half in returned:
        total = jnp.dot(mixing_hi, half, preferred_element_type=jnp.float32)
        sums.append(total + jnp.dot(mixing_lo, half, preferred_element_type=jnp.float32))
    expert_sum = jnp.concatenate(sums, axis=1)
    expert_sum = jnp.where(me == 0, expert_sum, jnp.roll(expert_sum, part_cols, axis=1))
    new_state = (summed.astype(jnp.float32) + expert_sum).astype(jnp.bfloat16)
    normed_state = rms_scale(new_state, post_gain).astype(jnp.bfloat16)
    return (new_state, normed_state)


def solution(mesh):
    return jax.shard_map(
        per_device,
        mesh=mesh,
        in_specs=(
            P(("ep", "dp"), None),
            P(("ep", "dp"), None),
            P(None, "dp"),
            P(),
            P(("ep", "dp"), None),
            P(("ep", "dp"), None),
            P("ep", None, "dp"),
            P("ep", None, "dp"),
            P("ep", None, "dp"),
            P(),
        ),
        out_specs=(P(("ep", "dp"), None), P(("ep", "dp"), None)),
        check_vma=False,
    )
```

```python
import jax
import jax.numpy as jnp
from jax import lax
from jax.sharding import PartitionSpec as P


def rms_scale(values, gain):
    widened = values.astype(jnp.float32)
    meansq = jnp.mean(widened * widened, axis=-1, keepdims=True)
    return widened * lax.rsqrt(meansq + 1e-06) * gain


def slot_table(route_block, experts, capacity):
    flat_ids = route_block.reshape(-1)
    onehot = (flat_ids[:, None] == jnp.arange(experts, dtype=jnp.int32)[None, :]).astype(jnp.int32)
    before = jnp.cumsum(onehot, axis=0) - onehot
    rank_in = jnp.sum(before * onehot, axis=1)
    return (flat_ids * capacity + rank_in).reshape(route_block.shape)


def exchange_rows(rows, experts):
    total, width = rows.shape
    lanes = 128
    wire = rows.reshape(experts, total * width // (experts * lanes), lanes)
    moved = lax.all_to_all(wire, "ep", split_axis=0, concat_axis=0, tiled=True)
    return moved.reshape(total, width)


def per_device(
    attention_out,
    residual,
    out_weight,
    pre_gain,
    routes,
    gate_prob,
    gate_weight,
    up_weight,
    down_weight,
    post_gain,
):
    groups = lax.axis_size("dp")
    experts = lax.axis_size("ep")
    tok_rows, top_picks = routes.shape
    row_width = residual.shape[1]
    part_cols = out_weight.shape[1]
    capacity = max(2, 3 * tok_rows * top_picks // (2 * experts))
    swap = [(0, 1), (1, 0)]
    me = lax.axis_index("dp")
    partner_att = lax.ppermute(attention_out, "dp", swap)
    cols = jnp.dot(
        jnp.concatenate([attention_out, partner_att], axis=0),
        out_weight,
        preferred_element_type=jnp.float32,
    )
    cols_own, cols_partner = cols[:tok_rows], cols[tok_rows:]
    cols_in = lax.ppermute(cols_partner.astype(jnp.bfloat16), "dp", swap).astype(jnp.float32)
    home_cols = jnp.where(
        me == 0,
        jnp.concatenate([cols_own, cols_in], axis=1),
        jnp.concatenate([cols_in, cols_own], axis=1),
    )
    summed = (residual.astype(jnp.float32) + home_cols).astype(jnp.bfloat16)
    normed_in = rms_scale(summed, pre_gain).astype(jnp.bfloat16)
    slot_ids = slot_table(routes, experts, capacity)
    matches = (
        slot_ids[:, :, None] == jnp.arange(experts * capacity, dtype=jnp.int32)[None, None, :]
    ).astype(jnp.float32)
    placing = jnp.sum(matches, axis=1).astype(jnp.bfloat16)
    weights = gate_prob / jnp.sum(gate_prob, axis=1, keepdims=True)
    mixing = jnp.sum(weights[:, :, None] * matches, axis=1)
    outgoing = lax.dot_general(
        placing, normed_in, (((0,), (0,)), ((), ())), preferred_element_type=jnp.float32
    ).astype(jnp.bfloat16)
    gate_local = gate_weight[0]
    up_local = up_weight[0]
    down_local = down_weight[0]
    own_rows = exchange_rows(outgoing, experts)
    other_rows = lax.ppermute(own_rows, "dp", swap)

    def hidden_of(rows):
        gate_part = jnp.dot(rows, gate_local, preferred_element_type=jnp.float32)
        up_part = jnp.dot(rows, up_local, preferred_element_type=jnp.float32)
        return (jax.nn.silu(gate_part) * up_part).astype(jnp.bfloat16)

    hidden_own = hidden_of(own_rows)
    hidden_own_in = lax.ppermute(hidden_own, "dp", swap)
    hidden_other = hidden_of(other_rows)
    hidden_other_in = lax.ppermute(hidden_other, "dp", swap)
    me = lax.axis_index("dp")

    ff_half = hidden_own.shape[1]
    down_mine = lax.dynamic_slice_in_dim(down_local, me * ff_half, ff_half, axis=0)
    down_theirs = lax.dynamic_slice_in_dim(down_local, (1 - me) * ff_half, ff_half, axis=0)

    def project(mine, theirs):
        total = jnp.dot(mine, down_mine, preferred_element_type=jnp.float32)
        total = total + jnp.dot(theirs, down_theirs, preferred_element_type=jnp.float32)
        return total.astype(jnp.bfloat16)

    out_other = project(hidden_other, hidden_own_in)
    out_other_in = lax.ppermute(out_other, "dp", swap)
    out_own = project(hidden_own, hidden_other_in)
    joined = jnp.concatenate([out_own, out_other_in], axis=1)
    returned = exchange_rows(joined, experts)
    mixing_hi = mixing.astype(jnp.bfloat16)
    mixing_lo = (mixing - mixing_hi.astype(jnp.float32)).astype(jnp.bfloat16)
    expert_sum = jnp.dot(mixing_hi, returned, preferred_element_type=jnp.float32)
    expert_sum = expert_sum + jnp.dot(mixing_lo, returned, preferred_element_type=jnp.float32)
    expert_sum = jnp.where(me == 0, expert_sum, jnp.roll(expert_sum, part_cols, axis=1))
    new_state = (summed.astype(jnp.float32) + expert_sum).astype(jnp.bfloat16)
    normed_state = rms_scale(new_state, post_gain).astype(jnp.bfloat16)
    return (new_state, normed_state)


def solution(mesh):
    return jax.shard_map(
        per_device,
        mesh=mesh,
        in_specs=(
            P(("ep", "dp"), None),
            P(("ep", "dp"), None),
            P(None, "dp"),
            P(),
            P(("ep", "dp"), None),
            P(("ep", "dp"), None),
            P("ep", None, "dp"),
            P("ep", None, "dp"),
            P("ep", None, "dp"),
            P(),
        ),
        out_specs=(P(("ep", "dp"), None), P(("ep", "dp"), None)),
        check_vma=False,
    )
```

```python
import jax
import jax.numpy as jnp
from jax import lax
from jax.sharding import PartitionSpec as P


def rms_scale(values, gain):
    widened = values.astype(jnp.float32)
    meansq = jnp.mean(widened * widened, axis=-1, keepdims=True)
    return widened * lax.rsqrt(meansq + 1e-06) * gain


def slot_table(route_block, experts, capacity):
    flat_ids = route_block.reshape(-1)
    onehot = (flat_ids[:, None] == jnp.arange(experts, dtype=jnp.int32)[None, :]).astype(jnp.int32)
    before = jnp.cumsum(onehot, axis=0) - onehot
    rank_in = jnp.sum(before * onehot, axis=1)
    return (flat_ids * capacity + rank_in).reshape(route_block.shape)


def exchange_rows(rows, experts):
    total, width = rows.shape
    lanes = 128
    wire = rows.reshape(experts, total * width // (experts * lanes), lanes)
    moved = lax.all_to_all(wire, "ep", split_axis=0, concat_axis=0, tiled=True)
    return moved.reshape(total, width)


def per_device(
    attention_out,
    residual,
    out_weight,
    pre_gain,
    routes,
    gate_prob,
    gate_weight,
    up_weight,
    down_weight,
    post_gain,
):
    groups = lax.axis_size("dp")
    experts = lax.axis_size("ep")
    tok_rows, top_picks = routes.shape
    row_width = residual.shape[1]
    part_cols = out_weight.shape[1]
    capacity = max(2, 3 * tok_rows * top_picks // (2 * experts))
    swap = [(0, 1), (1, 0)]
    me = lax.axis_index("dp")
    gate_local = gate_weight[0]
    up_local = up_weight[0]
    down_local = down_weight[0]
    gate_partner = lax.ppermute(gate_local, "dp", swap)
    up_partner = lax.ppermute(up_local, "dp", swap)
    down_partner = lax.ppermute(down_local, "dp", swap)
    partner_att = lax.ppermute(attention_out, "dp", swap)
    cols = jnp.dot(
        jnp.concatenate([attention_out, partner_att], axis=0),
        out_weight,
        preferred_element_type=jnp.float32,
    )
    cols_own, cols_partner = cols[:tok_rows], cols[tok_rows:]
    cols_in = lax.ppermute(cols_partner.astype(jnp.bfloat16), "dp", swap).astype(jnp.float32)
    home_cols = jnp.where(
        me == 0,
        jnp.concatenate([cols_own, cols_in], axis=1),
        jnp.concatenate([cols_in, cols_own], axis=1),
    )
    summed = (residual.astype(jnp.float32) + home_cols).astype(jnp.bfloat16)
    normed_in = rms_scale(summed, pre_gain).astype(jnp.bfloat16)
    slot_ids = slot_table(routes, experts, capacity)
    matches = (
        slot_ids[:, :, None] == jnp.arange(experts * capacity, dtype=jnp.int32)[None, None, :]
    ).astype(jnp.float32)
    placing = jnp.sum(matches, axis=1).astype(jnp.bfloat16)
    weights = gate_prob / jnp.sum(gate_prob, axis=1, keepdims=True)
    mixing = jnp.sum(weights[:, :, None] * matches, axis=1)
    outgoing = lax.dot_general(
        placing, normed_in, (((0,), (0,)), ((), ())), preferred_element_type=jnp.float32
    ).astype(jnp.bfloat16)
    own_rows = exchange_rows(outgoing, experts)
    me = lax.axis_index("dp")
    ff_half = gate_local.shape[1]

    def hidden_of(rows, gate_w, up_w):
        gate_part = jnp.dot(rows, gate_w, preferred_element_type=jnp.float32)
        up_part = jnp.dot(rows, up_w, preferred_element_type=jnp.float32)
        return (jax.nn.silu(gate_part) * up_part).astype(jnp.bfloat16)

    def project(mine, theirs, down_w):
        first = lax.dynamic_slice_in_dim(down_w, me * ff_half, ff_half, axis=0)
        second = lax.dynamic_slice_in_dim(down_w, (1 - me) * ff_half, ff_half, axis=0)
        total = jnp.dot(mine, first, preferred_element_type=jnp.float32)
        total = total + jnp.dot(theirs, second, preferred_element_type=jnp.float32)
        return total.astype(jnp.bfloat16)

    hidden_mine = hidden_of(own_rows, gate_local, up_local)
    hidden_theirs = hidden_of(own_rows, gate_partner, up_partner)
    out_own = project(hidden_mine, hidden_theirs, down_local)
    out_other = project(hidden_mine, hidden_theirs, down_partner)
    joined = jnp.concatenate([out_own, out_other], axis=1)
    returned = exchange_rows(joined, experts)
    mixing_hi = mixing.astype(jnp.bfloat16)
    mixing_lo = (mixing - mixing_hi.astype(jnp.float32)).astype(jnp.bfloat16)
    expert_sum = jnp.dot(mixing_hi, returned, preferred_element_type=jnp.float32)
    expert_sum = expert_sum + jnp.dot(mixing_lo, returned, preferred_element_type=jnp.float32)
    expert_sum = jnp.where(me == 0, expert_sum, jnp.roll(expert_sum, part_cols, axis=1))
    new_state = (summed.astype(jnp.float32) + expert_sum).astype(jnp.bfloat16)
    normed_state = rms_scale(new_state, post_gain).astype(jnp.bfloat16)
    return (new_state, normed_state)


def solution(mesh):
    return jax.shard_map(
        per_device,
        mesh=mesh,
        in_specs=(
            P(("ep", "dp"), None),
            P(("ep", "dp"), None),
            P(None, "dp"),
            P(),
            P(("ep", "dp"), None),
            P(("ep", "dp"), None),
            P("ep", None, "dp"),
            P("ep", None, "dp"),
            P("ep", None, "dp"),
            P(),
        ),
        out_specs=(P(("ep", "dp"), None), P(("ep", "dp"), None)),
        check_vma=False,
    )
```

```python
import jax
import jax.numpy as jnp
from jax import lax
from jax.sharding import PartitionSpec as P


def rms_scale(values, gain):
    widened = values.astype(jnp.float32)
    meansq = jnp.mean(widened * widened, axis=-1, keepdims=True)
    return widened * lax.rsqrt(meansq + 1e-06) * gain


def slot_table(route_block, experts, capacity):
    flat_ids = route_block.reshape(-1)
    onehot = (flat_ids[:, None] == jnp.arange(experts, dtype=jnp.int32)[None, :]).astype(jnp.int32)
    before = jnp.cumsum(onehot, axis=0) - onehot
    rank_in = jnp.sum(before * onehot, axis=1)
    return (flat_ids * capacity + rank_in).reshape(route_block.shape)


def exchange_rows(rows, experts):
    total, width = rows.shape
    lanes = 128
    wire = rows.reshape(experts, total * width // (experts * lanes), lanes)
    moved = lax.all_to_all(wire, "ep", split_axis=0, concat_axis=0, tiled=True)
    return moved.reshape(total, width)


def per_device(
    attention_out,
    residual,
    out_weight,
    pre_gain,
    routes,
    gate_prob,
    gate_weight,
    up_weight,
    down_weight,
    post_gain,
):
    groups = lax.axis_size("dp")
    experts = lax.axis_size("ep")
    tok_rows, top_picks = routes.shape
    row_width = residual.shape[1]
    part_cols = out_weight.shape[1]
    capacity = max(2, 3 * tok_rows * top_picks // (2 * experts))
    swap = [(0, 1), (1, 0)]
    me = lax.axis_index("dp")
    gate_local = gate_weight[0]
    up_local = up_weight[0]
    down_local = down_weight[0]
    gate_partner = lax.ppermute(gate_local, "dp", swap)
    up_partner = lax.ppermute(up_local, "dp", swap)
    down_partner = lax.ppermute(down_local, "dp", swap)
    partner_att = lax.ppermute(attention_out, "dp", swap)
    cols = jnp.dot(
        jnp.concatenate([attention_out, partner_att], axis=0),
        out_weight,
        preferred_element_type=jnp.float32,
    )
    cols_own, cols_partner = cols[:tok_rows], cols[tok_rows:]
    cols_in = lax.ppermute(cols_partner.astype(jnp.bfloat16), "dp", swap).astype(jnp.float32)
    home_cols = jnp.where(
        me == 0,
        jnp.concatenate([cols_own, cols_in], axis=1),
        jnp.concatenate([cols_in, cols_own], axis=1),
    )
    summed = (residual.astype(jnp.float32) + home_cols).astype(jnp.bfloat16)
    normed_in = rms_scale(summed, pre_gain).astype(jnp.bfloat16)
    slot_ids = slot_table(routes, experts, capacity)
    matches = (
        slot_ids[:, :, None] == jnp.arange(experts * capacity, dtype=jnp.int32)[None, None, :]
    ).astype(jnp.float32)
    placing = jnp.sum(matches, axis=1).astype(jnp.bfloat16)
    weights = gate_prob / jnp.sum(gate_prob, axis=1, keepdims=True)
    mixing = jnp.sum(weights[:, :, None] * matches, axis=1)
    outgoing = lax.dot_general(
        placing, normed_in, (((0,), (0,)), ((), ())), preferred_element_type=jnp.float32
    ).astype(jnp.bfloat16)
    own_rows = exchange_rows(outgoing, experts)
    me = lax.axis_index("dp")
    ff_half = gate_local.shape[1]

    def hidden_of(rows, gate_w, up_w):
        gate_part = jnp.dot(rows, gate_w, preferred_element_type=jnp.float32)
        up_part = jnp.dot(rows, up_w, preferred_element_type=jnp.float32)
        return (jax.nn.silu(gate_part) * up_part).astype(jnp.bfloat16)

    hidden_mine = hidden_of(own_rows, gate_local, up_local)
    hidden_theirs = hidden_of(own_rows, gate_partner, up_partner)
    hidden_full = jnp.where(
        me == 0,
        jnp.concatenate([hidden_mine, hidden_theirs], axis=1),
        jnp.concatenate([hidden_theirs, hidden_mine], axis=1),
    )
    out_own = jnp.dot(hidden_full, down_local, preferred_element_type=jnp.float32).astype(jnp.bfloat16)
    out_other = jnp.dot(hidden_full, down_partner, preferred_element_type=jnp.float32).astype(
        jnp.bfloat16
    )
    joined = jnp.concatenate([out_own, out_other], axis=1)
    returned = exchange_rows(joined, experts)
    mixing_hi = mixing.astype(jnp.bfloat16)
    mixing_lo = (mixing - mixing_hi.astype(jnp.float32)).astype(jnp.bfloat16)
    expert_sum = jnp.dot(mixing_hi, returned, preferred_element_type=jnp.float32)
    expert_sum = expert_sum + jnp.dot(mixing_lo, returned, preferred_element_type=jnp.float32)
    expert_sum = jnp.where(me == 0, expert_sum, jnp.roll(expert_sum, part_cols, axis=1))
    new_state = (summed.astype(jnp.float32) + expert_sum).astype(jnp.bfloat16)
    normed_state = rms_scale(new_state, post_gain).astype(jnp.bfloat16)
    return (new_state, normed_state)


def solution(mesh):
    return jax.shard_map(
        per_device,
        mesh=mesh,
        in_specs=(
            P(("ep", "dp"), None),
            P(("ep", "dp"), None),
            P(None, "dp"),
            P(),
            P(("ep", "dp"), None),
            P(("ep", "dp"), None),
            P("ep", None, "dp"),
            P("ep", None, "dp"),
            P("ep", None, "dp"),
            P(),
        ),
        out_specs=(P(("ep", "dp"), None), P(("ep", "dp"), None)),
        check_vma=False,
    )
```

```python
import jax
import jax.numpy as jnp
from jax import lax
from jax.sharding import PartitionSpec as P


def rms_scale(values, gain):
    widened = values.astype(jnp.float32)
    meansq = jnp.mean(widened * widened, axis=-1, keepdims=True)
    return widened * lax.rsqrt(meansq + 1e-06) * gain


def slot_table(route_block, experts, capacity):
    flat_ids = route_block.reshape(-1)
    onehot = (flat_ids[:, None] == jnp.arange(experts, dtype=jnp.int32)[None, :]).astype(jnp.int32)
    before = jnp.cumsum(onehot, axis=0) - onehot
    rank_in = jnp.sum(before * onehot, axis=1)
    return (flat_ids * capacity + rank_in).reshape(route_block.shape)


def exchange_rows(rows, experts):
    total, width = rows.shape
    lanes = 128
    wire = rows.reshape(experts, total * width // (experts * lanes), lanes)
    moved = lax.all_to_all(wire, "ep", split_axis=0, concat_axis=0, tiled=True)
    return moved.reshape(total, width)


def per_device(
    attention_out,
    residual,
    out_weight,
    pre_gain,
    routes,
    gate_prob,
    gate_weight,
    up_weight,
    down_weight,
    post_gain,
):
    groups = lax.axis_size("dp")
    experts = lax.axis_size("ep")
    tok_rows, top_picks = routes.shape
    row_width = residual.shape[1]
    part_cols = out_weight.shape[1]
    capacity = max(2, 3 * tok_rows * top_picks // (2 * experts))
    swap = [(0, 1), (1, 0)]
    me = lax.axis_index("dp")
    gate_local = gate_weight[0]
    up_local = up_weight[0]
    down_local = down_weight[0]
    gate_partner = lax.ppermute(gate_local, "dp", swap)
    up_partner = lax.ppermute(up_local, "dp", swap)
    down_partner = lax.ppermute(down_local, "dp", swap)
    partner_att = lax.ppermute(attention_out, "dp", swap)
    cols = jnp.dot(
        jnp.concatenate([attention_out, partner_att], axis=0),
        out_weight,
        preferred_element_type=jnp.float32,
    )
    cols_own, cols_partner = cols[:tok_rows], cols[tok_rows:]
    cols_in = lax.ppermute(cols_partner.astype(jnp.bfloat16), "dp", swap).astype(jnp.float32)
    home_cols = jnp.where(
        me == 0,
        jnp.concatenate([cols_own, cols_in], axis=1),
        jnp.concatenate([cols_in, cols_own], axis=1),
    )
    summed = (residual.astype(jnp.float32) + home_cols).astype(jnp.bfloat16)
    normed_in = rms_scale(summed, pre_gain).astype(jnp.bfloat16)
    slot_ids = slot_table(routes, experts, capacity)
    matches = (
        slot_ids[:, :, None] == jnp.arange(experts * capacity, dtype=jnp.int32)[None, None, :]
    ).astype(jnp.float32)
    placing = jnp.sum(matches, axis=1).astype(jnp.bfloat16)
    weights = gate_prob / jnp.sum(gate_prob, axis=1, keepdims=True)
    mixing = jnp.sum(weights[:, :, None] * matches, axis=1)
    outgoing = lax.dot_general(
        placing, normed_in, (((0,), (0,)), ((), ())), preferred_element_type=jnp.float32
    ).astype(jnp.bfloat16)
    own_rows = exchange_rows(outgoing, experts)
    me = lax.axis_index("dp")
    ff_half = gate_local.shape[1]

    def hidden_of(rows, gate_w, up_w):
        gate_part = jnp.dot(rows, gate_w, preferred_element_type=jnp.float32)
        up_part = jnp.dot(rows, up_w, preferred_element_type=jnp.float32)
        return (jax.nn.silu(gate_part) * up_part).astype(jnp.bfloat16)

    hidden_mine = hidden_of(own_rows, gate_local, up_local)
    hidden_theirs = hidden_of(own_rows, gate_partner, up_partner)
    hidden_full = jnp.where(
        me == 0,
        jnp.concatenate([hidden_mine, hidden_theirs], axis=1),
        jnp.concatenate([hidden_theirs, hidden_mine], axis=1),
    )
    joined = jnp.dot(
        hidden_full,
        jnp.concatenate([down_local, down_partner], axis=1),
        preferred_element_type=jnp.float32,
    ).astype(jnp.bfloat16)
    returned = exchange_rows(joined, experts)
    mixing_hi = mixing.astype(jnp.bfloat16)
    mixing_lo = (mixing - mixing_hi.astype(jnp.float32)).astype(jnp.bfloat16)
    expert_sum = jnp.dot(mixing_hi, returned, preferred_element_type=jnp.float32)
    expert_sum = expert_sum + jnp.dot(mixing_lo, returned, preferred_element_type=jnp.float32)
    expert_sum = jnp.where(me == 0, expert_sum, jnp.roll(expert_sum, part_cols, axis=1))
    new_state = (summed.astype(jnp.float32) + expert_sum).astype(jnp.bfloat16)
    normed_state = rms_scale(new_state, post_gain).astype(jnp.bfloat16)
    return (new_state, normed_state)


def solution(mesh):
    return jax.shard_map(
        per_device,
        mesh=mesh,
        in_specs=(
            P(("ep", "dp"), None),
            P(("ep", "dp"), None),
            P(None, "dp"),
            P(),
            P(("ep", "dp"), None),
            P(("ep", "dp"), None),
            P("ep", None, "dp"),
            P("ep", None, "dp"),
            P("ep", None, "dp"),
            P(),
        ),
        out_specs=(P(("ep", "dp"), None), P(("ep", "dp"), None)),
        check_vma=False,
    )
```

```python
import jax
import jax.numpy as jnp
from jax import lax
from jax.sharding import PartitionSpec as P


def rms_scale(values, gain):
    widened = values.astype(jnp.float32)
    meansq = jnp.mean(widened * widened, axis=-1, keepdims=True)
    return widened * lax.rsqrt(meansq + 1e-06) * gain


def slot_table(route_block, experts, capacity):
    flat_ids = route_block.reshape(-1)
    onehot = (flat_ids[:, None] == jnp.arange(experts, dtype=jnp.int32)[None, :]).astype(jnp.int32)
    before = jnp.cumsum(onehot, axis=0) - onehot
    rank_in = jnp.sum(before * onehot, axis=1)
    return (flat_ids * capacity + rank_in).reshape(route_block.shape)


def exchange_rows(rows, experts):
    total, width = rows.shape
    lanes = 128
    wire = rows.reshape(experts, total * width // (experts * lanes), lanes)
    moved = lax.all_to_all(wire, "ep", split_axis=0, concat_axis=0, tiled=True)
    return moved.reshape(total, width)


def per_device(
    attention_out,
    residual,
    out_weight,
    pre_gain,
    routes,
    gate_prob,
    gate_weight,
    up_weight,
    down_weight,
    post_gain,
):
    groups = lax.axis_size("dp")
    experts = lax.axis_size("ep")
    tok_rows, top_picks = routes.shape
    row_width = residual.shape[1]
    part_cols = out_weight.shape[1]
    capacity = max(2, 3 * tok_rows * top_picks // (2 * experts))
    swap = [(0, 1), (1, 0)]
    me = lax.axis_index("dp")
    gate_local = gate_weight[0]
    up_local = up_weight[0]
    down_local = down_weight[0]
    gate_partner = lax.ppermute(gate_local, "dp", swap)
    up_partner = lax.ppermute(up_local, "dp", swap)
    down_partner = lax.ppermute(down_local, "dp", swap)
    partner_att = lax.ppermute(attention_out, "dp", swap)
    cols = jnp.dot(
        jnp.concatenate([attention_out, partner_att], axis=0),
        out_weight,
        preferred_element_type=jnp.float32,
    )
    cols_own, cols_partner = cols[:tok_rows], cols[tok_rows:]
    cols_in = lax.ppermute(cols_partner.astype(jnp.bfloat16), "dp", swap).astype(jnp.float32)
    home_cols = jnp.where(
        me == 0,
        jnp.concatenate([cols_own, cols_in], axis=1),
        jnp.concatenate([cols_in, cols_own], axis=1),
    )
    summed = (residual.astype(jnp.float32) + home_cols).astype(jnp.bfloat16)
    normed_in = rms_scale(summed, pre_gain).astype(jnp.bfloat16)
    slot_ids = slot_table(routes, experts, capacity)
    matches = (
        slot_ids[:, :, None] == jnp.arange(experts * capacity, dtype=jnp.int32)[None, None, :]
    ).astype(jnp.float32)
    placing = jnp.sum(matches, axis=1).astype(jnp.bfloat16)
    weights = gate_prob / jnp.sum(gate_prob, axis=1, keepdims=True)
    mixing = jnp.sum(weights[:, :, None] * matches, axis=1)
    outgoing = lax.dot_general(
        placing, normed_in, (((0,), (0,)), ((), ())), preferred_element_type=jnp.float32
    ).astype(jnp.bfloat16)
    own_rows = exchange_rows(outgoing, experts)
    me = lax.axis_index("dp")
    ff_half = gate_local.shape[1]

    def hidden_of(rows, gate_w, up_w):
        gate_part = jnp.dot(rows, gate_w, preferred_element_type=jnp.float32)
        up_part = jnp.dot(rows, up_w, preferred_element_type=jnp.float32)
        return (jax.nn.silu(gate_part) * up_part).astype(jnp.bfloat16)

    hidden_pair = hidden_of(
        own_rows,
        jnp.concatenate([gate_local, gate_partner], axis=1),
        jnp.concatenate([up_local, up_partner], axis=1),
    )
    swapped = jnp.concatenate([hidden_pair[:, ff_half:], hidden_pair[:, :ff_half]], axis=1)
    hidden_full = jnp.where(me == 0, hidden_pair, swapped)
    joined = jnp.dot(
        hidden_full,
        jnp.concatenate([down_local, down_partner], axis=1),
        preferred_element_type=jnp.float32,
    ).astype(jnp.bfloat16)
    returned = exchange_rows(joined, experts)
    mixing_hi = mixing.astype(jnp.bfloat16)
    mixing_lo = (mixing - mixing_hi.astype(jnp.float32)).astype(jnp.bfloat16)
    expert_sum = jnp.dot(mixing_hi, returned, preferred_element_type=jnp.float32)
    expert_sum = expert_sum + jnp.dot(mixing_lo, returned, preferred_element_type=jnp.float32)
    expert_sum = jnp.where(me == 0, expert_sum, jnp.roll(expert_sum, part_cols, axis=1))
    new_state = (summed.astype(jnp.float32) + expert_sum).astype(jnp.bfloat16)
    normed_state = rms_scale(new_state, post_gain).astype(jnp.bfloat16)
    return (new_state, normed_state)


def solution(mesh):
    return jax.shard_map(
        per_device,
        mesh=mesh,
        in_specs=(
            P(("ep", "dp"), None),
            P(("ep", "dp"), None),
            P(None, "dp"),
            P(),
            P(("ep", "dp"), None),
            P(("ep", "dp"), None),
            P("ep", None, "dp"),
            P("ep", None, "dp"),
            P("ep", None, "dp"),
            P(),
        ),
        out_specs=(P(("ep", "dp"), None), P(("ep", "dp"), None)),
        check_vma=False,
    )
```

```python
import jax
import jax.numpy as jnp
from jax import lax
from jax.sharding import PartitionSpec as P


def rms_scale(values, gain):
    widened = values.astype(jnp.float32)
    meansq = jnp.mean(widened * widened, axis=-1, keepdims=True)
    return widened * lax.rsqrt(meansq + 1e-06) * gain


def slot_table(route_block, experts, capacity):
    flat_ids = route_block.reshape(-1)
    onehot = (flat_ids[:, None] == jnp.arange(experts, dtype=jnp.int32)[None, :]).astype(jnp.int32)
    before = jnp.cumsum(onehot, axis=0) - onehot
    rank_in = jnp.sum(before * onehot, axis=1)
    return (flat_ids * capacity + rank_in).reshape(route_block.shape)


def exchange_rows(rows, experts):
    total, width = rows.shape
    lanes = 128
    wire = rows.reshape(experts, total * width // (experts * lanes), lanes)
    moved = lax.all_to_all(wire, "ep", split_axis=0, concat_axis=0, tiled=True)
    return moved.reshape(total, width)


def per_device(
    attention_out,
    residual,
    out_weight,
    pre_gain,
    routes,
    gate_prob,
    gate_weight,
    up_weight,
    down_weight,
    post_gain,
):
    groups = lax.axis_size("dp")
    experts = lax.axis_size("ep")
    tok_rows, top_picks = routes.shape
    row_width = residual.shape[1]
    part_cols = out_weight.shape[1]
    capacity = max(2, 3 * tok_rows * top_picks // (2 * experts))
    swap = [(0, 1), (1, 0)]
    me = lax.axis_index("dp")
    gate_local = gate_weight[0]
    up_local = up_weight[0]
    down_local = down_weight[0]
    partner_att = lax.ppermute(attention_out, "dp", swap)
    cols = jnp.dot(
        jnp.concatenate([attention_out, partner_att], axis=0),
        out_weight,
        preferred_element_type=jnp.float32,
    )
    cols_own, cols_partner = cols[:tok_rows], cols[tok_rows:]
    cols_in = lax.ppermute(cols_partner.astype(jnp.bfloat16), "dp", swap).astype(jnp.float32)
    gate_send, up_send, down_send, cols_in = lax.optimization_barrier(
        (gate_local, up_local, down_local, cols_in)
    )
    gate_partner = lax.ppermute(gate_send, "dp", swap)
    up_partner = lax.ppermute(up_send, "dp", swap)
    down_partner = lax.ppermute(down_send, "dp", swap)
    home_cols = jnp.where(
        me == 0,
        jnp.concatenate([cols_own, cols_in], axis=1),
        jnp.concatenate([cols_in, cols_own], axis=1),
    )
    summed = (residual.astype(jnp.float32) + home_cols).astype(jnp.bfloat16)
    normed_in = rms_scale(summed, pre_gain).astype(jnp.bfloat16)
    slot_ids = slot_table(routes, experts, capacity)
    matches = (
        slot_ids[:, :, None] == jnp.arange(experts * capacity, dtype=jnp.int32)[None, None, :]
    ).astype(jnp.float32)
    placing = jnp.sum(matches, axis=1).astype(jnp.bfloat16)
    weights = gate_prob / jnp.sum(gate_prob, axis=1, keepdims=True)
    mixing = jnp.sum(weights[:, :, None] * matches, axis=1)
    outgoing = lax.dot_general(
        placing, normed_in, (((0,), (0,)), ((), ())), preferred_element_type=jnp.float32
    ).astype(jnp.bfloat16)
    own_rows = exchange_rows(outgoing, experts)
    me = lax.axis_index("dp")
    ff_half = gate_local.shape[1]

    def hidden_of(rows, gate_w, up_w):
        gate_part = jnp.dot(rows, gate_w, preferred_element_type=jnp.float32)
        up_part = jnp.dot(rows, up_w, preferred_element_type=jnp.float32)
        return (jax.nn.silu(gate_part) * up_part).astype(jnp.bfloat16)

    hidden_pair = hidden_of(
        own_rows,
        jnp.concatenate([gate_local, gate_partner], axis=1),
        jnp.concatenate([up_local, up_partner], axis=1),
    )
    swapped = jnp.concatenate([hidden_pair[:, ff_half:], hidden_pair[:, :ff_half]], axis=1)
    hidden_full = jnp.where(me == 0, hidden_pair, swapped)
    joined = jnp.dot(
        hidden_full,
        jnp.concatenate([down_local, down_partner], axis=1),
        preferred_element_type=jnp.float32,
    ).astype(jnp.bfloat16)
    returned = exchange_rows(joined, experts)
    mixing_hi = mixing.astype(jnp.bfloat16)
    mixing_lo = (mixing - mixing_hi.astype(jnp.float32)).astype(jnp.bfloat16)
    expert_sum = jnp.dot(mixing_hi, returned, preferred_element_type=jnp.float32)
    expert_sum = expert_sum + jnp.dot(mixing_lo, returned, preferred_element_type=jnp.float32)
    expert_sum = jnp.where(me == 0, expert_sum, jnp.roll(expert_sum, part_cols, axis=1))
    new_state = (summed.astype(jnp.float32) + expert_sum).astype(jnp.bfloat16)
    normed_state = rms_scale(new_state, post_gain).astype(jnp.bfloat16)
    return (new_state, normed_state)


def solution(mesh):
    return jax.shard_map(
        per_device,
        mesh=mesh,
        in_specs=(
            P(("ep", "dp"), None),
            P(("ep", "dp"), None),
            P(None, "dp"),
            P(),
            P(("ep", "dp"), None),
            P(("ep", "dp"), None),
            P("ep", None, "dp"),
            P("ep", None, "dp"),
            P("ep", None, "dp"),
            P(),
        ),
        out_specs=(P(("ep", "dp"), None), P(("ep", "dp"), None)),
        check_vma=False,
    )
```

```python
import jax
import jax.numpy as jnp
from jax import lax
from jax.sharding import PartitionSpec as P


def rms_scale(values, gain):
    widened = values.astype(jnp.float32)
    meansq = jnp.mean(widened * widened, axis=-1, keepdims=True)
    return widened * lax.rsqrt(meansq + 1e-06) * gain


def slot_table(route_block, experts, capacity):
    flat_ids = route_block.reshape(-1)
    onehot = (flat_ids[:, None] == jnp.arange(experts, dtype=jnp.int32)[None, :]).astype(jnp.int32)
    before = jnp.cumsum(onehot, axis=0) - onehot
    rank_in = jnp.sum(before * onehot, axis=1)
    return (flat_ids * capacity + rank_in).reshape(route_block.shape)


def exchange_rows(rows, experts):
    total, width = rows.shape
    lanes = 128
    wire = rows.reshape(experts, total * width // (experts * lanes), lanes)
    moved = lax.all_to_all(wire, "ep", split_axis=0, concat_axis=0, tiled=True)
    return moved.reshape(total, width)


def per_device(
    attention_out,
    residual,
    out_weight,
    pre_gain,
    routes,
    gate_prob,
    gate_weight,
    up_weight,
    down_weight,
    post_gain,
):
    groups = lax.axis_size("dp")
    experts = lax.axis_size("ep")
    tok_rows, top_picks = routes.shape
    row_width = residual.shape[1]
    part_cols = out_weight.shape[1]
    capacity = max(2, 3 * tok_rows * top_picks // (2 * experts))
    swap = [(0, 1), (1, 0)]
    me = lax.axis_index("dp")
    gate_local = gate_weight[0]
    up_local = up_weight[0]
    down_local = down_weight[0]
    partner_att = lax.ppermute(attention_out, "dp", swap)
    cols = jnp.dot(
        jnp.concatenate([attention_out, partner_att], axis=0),
        out_weight,
        preferred_element_type=jnp.float32,
    )
    cols_own, cols_partner = cols[:tok_rows], cols[tok_rows:]
    cols_in = lax.ppermute(cols_partner.astype(jnp.bfloat16), "dp", swap).astype(jnp.float32)
    gate_send, up_send, down_send, cols_in = lax.optimization_barrier(
        (gate_local, up_local, down_local, cols_in)
    )
    gate_partner = lax.ppermute(gate_send, "dp", swap)
    up_partner = lax.ppermute(up_send, "dp", swap)
    down_partner = lax.ppermute(down_send, "dp", swap)
    home_cols = jnp.where(
        me == 0,
        jnp.concatenate([cols_own, cols_in], axis=1),
        jnp.concatenate([cols_in, cols_own], axis=1),
    )
    summed = (residual.astype(jnp.float32) + home_cols).astype(jnp.bfloat16)
    normed_in = rms_scale(summed, pre_gain).astype(jnp.bfloat16)
    slot_ids = slot_table(routes, experts, capacity)
    matches = (
        slot_ids[:, :, None] == jnp.arange(experts * capacity, dtype=jnp.int32)[None, None, :]
    ).astype(jnp.float32)
    placing = jnp.sum(matches, axis=1).astype(jnp.bfloat16)
    weights = gate_prob / jnp.sum(gate_prob, axis=1, keepdims=True)
    mixing = jnp.sum(weights[:, :, None] * matches, axis=1)
    outgoing = lax.dot_general(
        placing, normed_in, (((0,), (0,)), ((), ())), preferred_element_type=jnp.float32
    ).astype(jnp.bfloat16)
    own_rows = exchange_rows(outgoing, experts)
    me = lax.axis_index("dp")
    ff_half = gate_local.shape[1]

    def hidden_of(rows, gate_w, up_w):
        gate_part = jnp.dot(rows, gate_w, preferred_element_type=jnp.float32)
        up_part = jnp.dot(rows, up_w, preferred_element_type=jnp.float32)
        return (jax.nn.silu(gate_part) * up_part).astype(jnp.bfloat16)

    hidden_pair = hidden_of(
        own_rows,
        jnp.concatenate([gate_local, gate_partner], axis=1),
        jnp.concatenate([up_local, up_partner], axis=1),
    )
    swapped = jnp.concatenate([hidden_pair[:, ff_half:], hidden_pair[:, :ff_half]], axis=1)
    hidden_full = jnp.where(me == 0, hidden_pair, swapped)
    joined = jnp.dot(
        hidden_full,
        jnp.concatenate([down_local, down_partner], axis=1),
        preferred_element_type=jnp.float32,
    ).astype(jnp.bfloat16)
    returned = exchange_rows(joined, experts)
    mixing_hi = mixing.astype(jnp.bfloat16)
    mixing_lo = (mixing - mixing_hi.astype(jnp.float32)).astype(jnp.bfloat16)
    expert_sum = jnp.dot(
        jnp.concatenate([mixing_hi, mixing_lo], axis=1),
        jnp.concatenate([returned, returned], axis=0),
        preferred_element_type=jnp.float32,
    )
    expert_sum = jnp.where(me == 0, expert_sum, jnp.roll(expert_sum, part_cols, axis=1))
    new_state = (summed.astype(jnp.float32) + expert_sum).astype(jnp.bfloat16)
    normed_state = rms_scale(new_state, post_gain).astype(jnp.bfloat16)
    return (new_state, normed_state)


def solution(mesh):
    return jax.shard_map(
        per_device,
        mesh=mesh,
        in_specs=(
            P(("ep", "dp"), None),
            P(("ep", "dp"), None),
            P(None, "dp"),
            P(),
            P(("ep", "dp"), None),
            P(("ep", "dp"), None),
            P("ep", None, "dp"),
            P("ep", None, "dp"),
            P("ep", None, "dp"),
            P(),
        ),
        out_specs=(P(("ep", "dp"), None), P(("ep", "dp"), None)),
        check_vma=False,
    )
```

```python
import jax
import jax.numpy as jnp
from jax import lax
from jax.sharding import PartitionSpec as P


def rms_scale(values, gain):
    widened = values.astype(jnp.float32)
    meansq = jnp.mean(widened * widened, axis=-1, keepdims=True)
    return widened * lax.rsqrt(meansq + 1e-06) * gain


def slot_table(route_block, experts, capacity):
    flat_ids = route_block.reshape(-1)
    onehot = (flat_ids[:, None] == jnp.arange(experts, dtype=jnp.int32)[None, :]).astype(jnp.int32)
    before = jnp.cumsum(onehot, axis=0) - onehot
    rank_in = jnp.sum(before * onehot, axis=1)
    return (flat_ids * capacity + rank_in).reshape(route_block.shape)


def exchange_rows(rows, experts):
    total, width = rows.shape
    lanes = 128
    wire = rows.reshape(experts, total * width // (experts * lanes), lanes)
    moved = lax.all_to_all(wire, "ep", split_axis=0, concat_axis=0, tiled=True)
    return moved.reshape(total, width)


def per_device(
    attention_out,
    residual,
    out_weight,
    pre_gain,
    routes,
    gate_prob,
    gate_weight,
    up_weight,
    down_weight,
    post_gain,
):
    groups = lax.axis_size("dp")
    experts = lax.axis_size("ep")
    tok_rows, top_picks = routes.shape
    row_width = residual.shape[1]
    part_cols = out_weight.shape[1]
    capacity = max(2, 3 * tok_rows * top_picks // (2 * experts))
    swap = [(0, 1), (1, 0)]
    me = lax.axis_index("dp")
    gate_local = gate_weight[0]
    up_local = up_weight[0]
    down_local = down_weight[0]
    partner_att = lax.ppermute(attention_out, "dp", swap)
    cols = jnp.dot(
        jnp.concatenate([attention_out, partner_att], axis=0),
        out_weight,
        preferred_element_type=jnp.float32,
    )
    cols_own, cols_partner = cols[:tok_rows], cols[tok_rows:]
    cols_in = lax.ppermute(cols_partner.astype(jnp.bfloat16), "dp", swap).astype(jnp.float32)
    home_cols = jnp.where(
        me == 0,
        jnp.concatenate([cols_own, cols_in], axis=1),
        jnp.concatenate([cols_in, cols_own], axis=1),
    )
    summed = (residual.astype(jnp.float32) + home_cols).astype(jnp.bfloat16)
    normed_in = rms_scale(summed, pre_gain).astype(jnp.bfloat16)
    slot_ids = slot_table(routes, experts, capacity)
    matches = (
        slot_ids[:, :, None] == jnp.arange(experts * capacity, dtype=jnp.int32)[None, None, :]
    ).astype(jnp.float32)
    placing = jnp.sum(matches, axis=1).astype(jnp.bfloat16)
    weights = gate_prob / jnp.sum(gate_prob, axis=1, keepdims=True)
    mixing = jnp.sum(weights[:, :, None] * matches, axis=1)
    outgoing = lax.dot_general(
        placing, normed_in, (((0,), (0,)), ((), ())), preferred_element_type=jnp.float32
    ).astype(jnp.bfloat16)
    gate_send, up_send, down_send, outgoing = lax.optimization_barrier(
        (gate_local, up_local, down_local, outgoing)
    )
    gate_partner = lax.ppermute(gate_send, "dp", swap)
    up_partner = lax.ppermute(up_send, "dp", swap)
    down_partner = lax.ppermute(down_send, "dp", swap)
    own_rows = exchange_rows(outgoing, experts)
    me = lax.axis_index("dp")
    ff_half = gate_local.shape[1]

    def hidden_of(rows, gate_w, up_w):
        gate_part = jnp.dot(rows, gate_w, preferred_element_type=jnp.float32)
        up_part = jnp.dot(rows, up_w, preferred_element_type=jnp.float32)
        return (jax.nn.silu(gate_part) * up_part).astype(jnp.bfloat16)

    hidden_pair = hidden_of(
        own_rows,
        jnp.concatenate([gate_local, gate_partner], axis=1),
        jnp.concatenate([up_local, up_partner], axis=1),
    )
    swapped = jnp.concatenate([hidden_pair[:, ff_half:], hidden_pair[:, :ff_half]], axis=1)
    hidden_full = jnp.where(me == 0, hidden_pair, swapped)
    joined = jnp.dot(
        hidden_full,
        jnp.concatenate([down_local, down_partner], axis=1),
        preferred_element_type=jnp.float32,
    ).astype(jnp.bfloat16)
    returned = exchange_rows(joined, experts)
    mixing_hi = mixing.astype(jnp.bfloat16)
    mixing_lo = (mixing - mixing_hi.astype(jnp.float32)).astype(jnp.bfloat16)
    expert_sum = jnp.dot(
        jnp.concatenate([mixing_hi, mixing_lo], axis=1),
        jnp.concatenate([returned, returned], axis=0),
        preferred_element_type=jnp.float32,
    )
    expert_sum = jnp.where(me == 0, expert_sum, jnp.roll(expert_sum, part_cols, axis=1))
    new_state = (summed.astype(jnp.float32) + expert_sum).astype(jnp.bfloat16)
    normed_state = rms_scale(new_state, post_gain).astype(jnp.bfloat16)
    return (new_state, normed_state)


def solution(mesh):
    return jax.shard_map(
        per_device,
        mesh=mesh,
        in_specs=(
            P(("ep", "dp"), None),
            P(("ep", "dp"), None),
            P(None, "dp"),
            P(),
            P(("ep", "dp"), None),
            P(("ep", "dp"), None),
            P("ep", None, "dp"),
            P("ep", None, "dp"),
            P("ep", None, "dp"),
            P(),
        ),
        out_specs=(P(("ep", "dp"), None), P(("ep", "dp"), None)),
        check_vma=False,
    )
```
